512 devices in a mesh: dir: 8 (over z_lo), row: 64 (over x, y, z_hi, core).
Axes of the slice: x: 4, y: 4, z: 16 (z_hi: 2, z_lo: 8; z = z_hi * 8 + z_lo), core: 2. Of those that a mesh axis runs over, the one named last changes fastest.
Arguments:
- white_noise: bfloat16 [2, 8192, 8192], P(None, ('dir', 'row')), may hold values from -6 to 6
- geometry: int32 [8, 2], P('dir'), may hold values from 0 to 3
- window: int32 [8], P('dir'), may hold values from 1 to 8, as said below
- tile_map: int32 [8, 8192], P('dir'), may hold values from 0 to 65535
- link_gain: float32 [8, 8192], P('dir'), may hold values from 0.1 to 1
- serving: int32 [8192], replicated, may hold values from 0 to 7
Outputs:
- fluctuation: float32 [8, 512, 128], P('dir', 'row')
- signal_ratio: float32 [8192], P(('dir', 'row'))
The draws below stay inside these ranges and needn't reach their ends.
Inputs may be any that keep to these rules, and one draw needn't show every extreme that they name: geometry[d,0] is direction d's Fresnel-scale bin and geometry[d,1] its slant bin. `window`: some direction has the half-width 8. `tile_map`: tile (t,u) is numbered t * 128 + u.
All inputs are finite; a program needn't handle non-finite values.
Results may differ from the reference program's by a relative error of at most 0.034.
Values may be sent and summed in bfloat16 or wider, within the bound.
No kernel may reach another device: no remote copies, remote signals or barrier semaphores. Data moves between devices by JAX's collectives and lax.ppermute only.
A program may use at most 64 MiB of HBM per device.

```python
import math
import jax
import jax.numpy as jnp
from jax import lax

N = 8192
FIRST = 64
SECOND = 128
ROWS_DEV = 32
PATCH = 2048
XTILES = 128
YTILES = 8
TILE_X = 64
TILE_Y = 4
WMAX = 8
DIRS = 8
GROUND = 8192
TILES = 65536
N_ROW = 64


def draw_window(key, part):
    values = jax.random.randint(key, (DIRS,), 1, WMAX + 1, dtype=jnp.int32)
    chosen_spot = jax.random.randint(jax.random.fold_in(key, 7), (), 0, DIRS, dtype=jnp.int32)
    return values.at[chosen_spot].set(WMAX)


def set_ends(result, rng, smallest, high):
    spot = [jax.random.randint(jax.random.fold_in(rng, axis), (), 0, length) for axis, length in enumerate(result.shape)]
    main_axis = result.shape.index(max(result.shape))
    beside = spot[:main_axis] + [(spot[main_axis] + 1) % result.shape[main_axis]] + spot[main_axis + 1:]
    return result.at[tuple(spot)].set(smallest).at[tuple(beside)].set(high)


def block_levels(stream_key, shape, split, smallest, largest):
    def one(axis_at, blocks):
        draws = jax.random.uniform(jax.random.fold_in(jax.random.fold_in(stream_key, 6), axis_at), (blocks,), jnp.float32, smallest / len(split), largest / len(split))
        return jnp.repeat(jnp.exp(draws), shape[axis_at] // blocks).reshape((-1,) + (1,) * (len(shape) - axis_at - 1))

    level = one(*split[0])
    for cut in split[1:]:
        level = level * one(*cut)
    return level


def noise(key, extent, scale, most, split=(), kind=jnp.bfloat16):
    factor_of = block_levels(key, extent, split, -0.22, 0.18) if split else 1.0
    values = jax.random.normal(key, extent, jnp.float32) * scale * factor_of
    return jnp.minimum(jnp.maximum(values, -most), most).astype(kind)


def setup_inputs(seed: int = 0) -> dict:
    keys = jax.random.split(jax.random.key(seed), 7)
    return {
        "white_noise": noise(keys[0], (2, N, N), 1.0, 6.0, ((1, 512),)),
        "geometry": set_ends(jax.random.randint(keys[1], (DIRS, 2), 0, 4), jax.random.fold_in(keys[1], 1), 0, 3).astype(jnp.int32),
        "window": draw_window(jax.random.fold_in(keys[6], 71), 0),
        "tile_map": set_ends(jax.random.randint(keys[3], (DIRS, GROUND), 0, TILES), jax.random.fold_in(keys[3], 1), 0, TILES - 1).astype(jnp.int32),
        "link_gain": jnp.clip(jnp.exp(math.log(1.0) - 2.3025851 * jax.random.uniform(keys[4], (DIRS, GROUND), jnp.float32) ** block_levels(keys[4], (DIRS, GROUND), ((0, 8),), -0.2, 0.2)), 0.1, 1.0),
        "serving": set_ends(jax.random.randint(keys[5], (GROUND,), 0, DIRS), jax.random.fold_in(keys[5], 1), 0, DIRS - 1).astype(jnp.int32),
    }


full_turn = 2.0 * math.pi
noise_floor = 0.05
tiny_value = 1e-6
strength = 1.6
row_patterns = ("zrab,zwak->wrkb", "zrkb,zwbc->wrkc", "zrkc,wzbc->wrkb", "zrkb,wzak->wrab", "zrkb,zak->rab")
column_patterns = ("zaby,zwak->wkby", "zkby,zwbc->wkcy", "zkcy,wzbc->wkby", "zkby,wzak->waby", "zkby,zak->aby")


def complex_block(real_part, imag_part):
    return jnp.stack([jnp.stack([real_part, imag_part]), jnp.stack([-imag_part, real_part])]).astype(jnp.bfloat16)


def transform_tables(first, second):
    total = first * second
    outer_ids = jnp.arange(first, dtype=jnp.int32)
    inner_ids = jnp.arange(second, dtype=jnp.int32)
    outer_angle = ((outer_ids[:, None] * outer_ids[None, :]) % first).astype(jnp.float32) * (full_turn / first)
    inner_angle = ((inner_ids[:, None] * inner_ids[None, :]) % second).astype(jnp.float32) * (full_turn / second)
    twist_angle = ((outer_ids[:, None] * inner_ids[None, :]) % total).astype(jnp.float32) * (full_turn / total)
    return (complex_block(jnp.cos(outer_angle), -jnp.sin(outer_angle)),
            complex_block(jnp.cos(inner_angle), -jnp.sin(inner_angle)),
            jnp.cos(twist_angle), -jnp.sin(twist_angle))


def signed_wave(positions, first, second):
    total = first * second
    wave_number = positions // second + first * (positions % second)
    return jnp.where(wave_number >= total // 2, wave_number - total, wave_number).astype(jnp.float32)


def spectral_filter(row_ids, column_ids):
    wave_rows = signed_wave(row_ids, FIRST, SECOND)
    wave_columns = signed_wave(column_ids, FIRST, SECOND)
    squared_radius = 16.0 + wave_rows[:, None] ** 2 + wave_columns[None, :] ** 2
    return strength * float(N) * float(N) * squared_radius ** -0.75


def fresnel_factor(geometry_row, first, second):
    total = first * second
    fresnel_area = 144.0 * jnp.exp2(geometry_row[0].astype(jnp.float32))
    positions = jnp.arange(total, dtype=jnp.int32).reshape(first, second)
    scaled = signed_wave(positions, first, second) * (full_turn / total)
    turning = 0.5 * scaled * scaled * fresnel_area
    return jnp.cos(turning), -jnp.sin(turning)


def complex_times(values, real_part, imag_part):
    return jnp.stack([values[0] * real_part - values[1] * imag_part, values[0] * imag_part + values[1] * real_part])


def contract(pattern, operand, matrix):
    return jnp.einsum(pattern, operand.astype(jnp.float32), matrix.astype(jnp.float32))


def table_length(tables):
    return tables[0].shape[2] * tables[1].shape[2]


def forward_axis(values, tables, factor, patterns, trailing):
    outer_table, inner_table, twist_real, twist_imag = tables
    factor_real, factor_imag = factor
    if trailing:
        twist_real, twist_imag = twist_real[..., None], twist_imag[..., None]
        factor_real, factor_imag = factor_real[..., None], factor_imag[..., None]
    section_one = complex_times(contract(patterns[0], values, outer_table), twist_real, twist_imag).astype(jnp.bfloat16)
    section_two = contract(patterns[1], section_one, inner_table)
    return complex_times(section_two, factor_real, factor_imag).astype(jnp.bfloat16)


def inverse_first(values, tables, patterns, trailing):
    outer_table, inner_table, twist_real, twist_imag = tables
    if trailing:
        twist_real, twist_imag = twist_real[..., None], twist_imag[..., None]
    return complex_times(contract(patterns[2], values, inner_table), twist_real, -twist_imag).astype(jnp.bfloat16)


def inverse_axis(values, tables, patterns, trailing):
    section_one = inverse_first(values, tables, patterns, trailing)
    return contract(patterns[3], section_one, tables[0]) * (1.0 / table_length(tables))


def inverse_real(values, tables, patterns, trailing):
    section_one = inverse_first(values, tables, patterns, trailing)
    return contract(patterns[4], section_one, tables[0][0]) * (1.0 / table_length(tables))


def window_matrix(half_width):
    positions = jnp.arange(XTILES, dtype=jnp.int32)
    difference = (positions[:, None] - positions[None, :]) % XTILES
    distance = jnp.minimum(difference, XTILES - difference)
    return (distance <= half_width).astype(jnp.float32)


def tile_statistics(first_moment, second_moment, half_width, tile_rows):
    window_mask = window_matrix(half_width)
    cells = ((2 * half_width + 1) * (TILE_X * tile_rows)).astype(jnp.float32)
    mean_one = jnp.dot(first_moment, window_mask, precision=lax.Precision.HIGHEST) / cells
    mean_two = jnp.dot(second_moment, window_mask, precision=lax.Precision.HIGHEST) / cells
    fluctuation = mean_two / (mean_one * mean_one + tiny_value) - 1.0
    return fluctuation, mean_one * jnp.exp(-fluctuation)


def reference(white_noise, geometry, window, tile_map, link_gain, serving):
    tables_x = transform_tables(FIRST, SECOND)
    tables_y = transform_tables(N_ROW, ROWS_DEV)
    all_ids = jnp.arange(N, dtype=jnp.int32)
    spectrum = (white_noise.astype(jnp.float32) * spectral_filter(all_ids, all_ids)).astype(jnp.bfloat16)
    half_screen = inverse_axis(spectrum.reshape(2, N, FIRST, SECOND), tables_x, row_patterns, False)
    half_screen = half_screen.astype(jnp.bfloat16).reshape(2, N, N)
    phase_screen = inverse_real(half_screen.reshape(2, FIRST, SECOND, N), tables_x, column_patterns, True).reshape(N, N)

    def one_direction(inputs):
        geometry_row, half_width, tile_row, gain_row, direction = inputs
        slant_factor = 1.0 + 0.25 * geometry_row[1].astype(jnp.float32)
        fresnel_x = fresnel_factor(geometry_row, FIRST, SECOND)
        fresnel_y = fresnel_factor(geometry_row, N_ROW, ROWS_DEV)
        offset_rows = (N // 4) * geometry_row[1]
        patch_ids = ((offset_rows + jnp.arange(PATCH, dtype=jnp.int32)) % N).astype(jnp.int32)
        patch = jnp.take(phase_screen, patch_ids, axis=0)
        turned_phase = slant_factor * patch
        screen_field = jnp.stack([jnp.cos(turned_phase), jnp.sin(turned_phase)]).astype(jnp.bfloat16)
        spectral = forward_axis(screen_field.reshape(2, N_ROW, ROWS_DEV, N), tables_y, fresnel_y, column_patterns, True)
        first_pass = inverse_axis(spectral, tables_y, column_patterns, True).astype(jnp.bfloat16).reshape(2, PATCH, N)
        spectral = forward_axis(first_pass.reshape(2, PATCH, FIRST, SECOND), tables_x, fresnel_x, row_patterns, False)
        wave_field = inverse_axis(spectral, tables_x, row_patterns, False).reshape(2, PATCH, N)
        intensity = wave_field[0] * wave_field[0] + wave_field[1] * wave_field[1]
        intensity = intensity.reshape(YTILES * N_ROW, TILE_Y, XTILES, TILE_X)
        first_moment = jnp.sum(intensity, axis=(1, 3))
        second_moment = jnp.sum(intensity * intensity, axis=(1, 3))
        fluctuation, faded_power = tile_statistics(first_moment, second_moment, half_width, TILE_Y)
        received = gain_row * jnp.take(faded_power.reshape(-1), tile_row)
        serves_here = serving == direction
        return fluctuation, jnp.where(serves_here, received, 0.0), jnp.where(serves_here, 0.0, received)

    direction_ids = jnp.arange(DIRS, dtype=jnp.int32)
    fluctuation, signal_parts, interference_parts = lax.map(
        one_direction, (geometry, window, tile_map, link_gain, direction_ids))
    signal = jnp.sum(signal_parts, axis=0)
    interference = jnp.sum(interference_parts, axis=0)
    signal_ratio = jnp.log10(signal / (interference + noise_floor))
    return fluctuation, signal_ratio
```

```python
import math

import jax
import jax.numpy as jnp
from jax import lax
from jax.sharding import PartitionSpec as P

N = 8192
FIRST = 64
SECOND = 128
ROWS_DEV = 32
XTILES = 128
YTILES = 8
TILE_X = 64


full_turn = 2.0 * math.pi
noise_floor = 0.05
tiny_value = 1e-06
strength = 1.6
row_patterns = (
    "zrab,zwak->wrkb",
    "zrkb,zwbc->wrkc",
    "zrkc,wzbc->wrkb",
    "zrkb,wzak->wrab",
    "zrkb,zak->rab",
)
column_patterns = (
    "zaby,zwak->wkby",
    "zkby,zwbc->wkcy",
    "zkcy,wzbc->wkby",
    "zkby,wzak->waby",
    "zkby,zak->aby",
)


def complex_block(real_part, imag_part):
    return jnp.stack(
        [jnp.stack([real_part, imag_part]), jnp.stack([-imag_part, real_part])]
    ).astype(jnp.bfloat16)


def transform_tables(first, second):
    total = first * second
    outer_ids = jnp.arange(first, dtype=jnp.int32)
    inner_ids = jnp.arange(second, dtype=jnp.int32)
    outer_angle = (outer_ids[:, None] * outer_ids[None, :] % first).astype(jnp.float32) * (
        full_turn / first
    )
    inner_angle = (inner_ids[:, None] * inner_ids[None, :] % second).astype(jnp.float32) * (
        full_turn / second
    )
    twist_angle = (outer_ids[:, None] * inner_ids[None, :] % total).astype(jnp.float32) * (
        full_turn / total
    )
    return (
        complex_block(jnp.cos(outer_angle), -jnp.sin(outer_angle)),
        complex_block(jnp.cos(inner_angle), -jnp.sin(inner_angle)),
        jnp.cos(twist_angle),
        -jnp.sin(twist_angle),
    )


def signed_wave(positions, first, second):
    total = first * second
    wave_number = positions // second + first * (positions % second)
    return jnp.where(wave_number >= total // 2, wave_number - total, wave_number).astype(
        jnp.float32
    )


def spectral_filter(row_ids, column_ids):
    wave_rows = signed_wave(row_ids, FIRST, SECOND)
    wave_columns = signed_wave(column_ids, FIRST, SECOND)
    squared_radius = 16.0 + wave_rows[:, None] ** 2 + wave_columns[None, :] ** 2
    return strength * float(N) * float(N) * squared_radius ** (-0.75)


def fresnel_factor(geometry_row, first, second):
    total = first * second
    fresnel_area = 144.0 * jnp.exp2(geometry_row[0].astype(jnp.float32))
    positions = jnp.arange(total, dtype=jnp.int32).reshape(first, second)
    scaled = signed_wave(positions, first, second) * (full_turn / total)
    turning = 0.5 * scaled * scaled * fresnel_area
    return (jnp.cos(turning), -jnp.sin(turning))


def complex_times(values, real_part, imag_part):
    return jnp.stack(
        [
            values[0] * real_part - values[1] * imag_part,
            values[0] * imag_part + values[1] * real_part,
        ]
    )


def contract(pattern, operand, matrix):
    return jnp.einsum(pattern, operand, matrix, preferred_element_type=jnp.float32)


def table_length(tables):
    return tables[0].shape[2] * tables[1].shape[2]


def forward_axis(values, tables, factor, patterns, trailing):
    outer_table, inner_table, twist_real, twist_imag = tables
    factor_real, factor_imag = factor
    if trailing:
        twist_real, twist_imag = (twist_real[..., None], twist_imag[..., None])
        factor_real, factor_imag = (factor_real[..., None], factor_imag[..., None])
    section_one = complex_times(
        contract(patterns[0], values, outer_table), twist_real, twist_imag
    ).astype(jnp.bfloat16)
    section_two = contract(patterns[1], section_one, inner_table)
    return complex_times(section_two, factor_real, factor_imag).astype(jnp.bfloat16)


def inverse_first(values, tables, patterns, trailing):
    outer_table, inner_table, twist_real, twist_imag = tables
    if trailing:
        twist_real, twist_imag = (twist_real[..., None], twist_imag[..., None])
    return complex_times(
        contract(patterns[2], values, inner_table), twist_real, -twist_imag
    ).astype(jnp.bfloat16)


def inverse_axis(values, tables, patterns, trailing):
    section_one = inverse_first(values, tables, patterns, trailing)
    return contract(patterns[3], section_one, tables[0]) * (1.0 / table_length(tables))


def window_matrix(half_width):
    positions = jnp.arange(XTILES, dtype=jnp.int32)
    difference = (positions[:, None] - positions[None, :]) % XTILES
    distance = jnp.minimum(difference, XTILES - difference)
    return (distance <= half_width).astype(jnp.float32)


def tile_statistics(first_moment, second_moment, half_width, tile_rows):
    window_mask = window_matrix(half_width)
    cells = ((2 * half_width + 1) * (TILE_X * tile_rows)).astype(jnp.float32)
    mean_one = jnp.dot(first_moment, window_mask, precision=lax.Precision.HIGHEST) / cells
    mean_two = jnp.dot(second_moment, window_mask, precision=lax.Precision.HIGHEST) / cells
    fluctuation = mean_two / (mean_one * mean_one + tiny_value) - 1.0
    return (fluctuation, mean_one * jnp.exp(-fluctuation))


def propagate_columns(phase_patch, tables_y, slant_factor, fresnel_y):
    patch_rows = phase_patch.shape[0]
    width_here = phase_patch.shape[1]
    outer_len = tables_y[0].shape[2]
    inner_len = tables_y[1].shape[2]
    turned_phase = slant_factor * phase_patch
    screen_field = jnp.stack([jnp.cos(turned_phase), jnp.sin(turned_phase)]).astype(jnp.bfloat16)
    stacked = screen_field.reshape(2, outer_len, inner_len, width_here)
    spectral = forward_axis(stacked, tables_y, fresnel_y, column_patterns, True)
    result = inverse_axis(spectral, tables_y, column_patterns, True)
    return result.astype(jnp.bfloat16).reshape(2, patch_rows, width_here)


def body(white_noise, geometry, window, tile_map, link_gain, serving):
    row_count = lax.axis_size("row")
    tables = transform_tables(FIRST, SECOND)
    tables_y = transform_tables(row_count, ROWS_DEV)
    patch_len = row_count * ROWS_DEV
    rows_here = white_noise.shape[1]
    row_start = lax.axis_index(("dir", "row")) * rows_here
    row_ids = row_start + jnp.arange(rows_here, dtype=jnp.int32)
    column_ids = jnp.arange(N, dtype=jnp.int32)
    spectral_gain = spectral_filter(row_ids, column_ids)
    spectrum = (white_noise.astype(jnp.float32) * spectral_gain).astype(jnp.bfloat16)
    half_screen = inverse_axis(
        spectrum.reshape(2, rows_here, FIRST, SECOND), tables, row_patterns, False
    )
    half_screen = half_screen.astype(jnp.bfloat16).reshape(2, rows_here, N)
    turned = lax.all_to_all(half_screen, "row", split_axis=2, concat_axis=1, tiled=True)
    band_rows = turned.shape[1]
    columns = turned.shape[2]
    slant_factor = 1.0 + 0.25 * geometry[0, 1].astype(jnp.float32)
    fresnel_x = fresnel_factor(geometry[0], FIRST, SECOND)
    fresnel_y = fresnel_factor(geometry[0], row_count, ROWS_DEV)
    offset_rows = N // 4 * geometry[0, 1]
    blocks = band_rows // SECOND
    block_start = lax.axis_index("dir") * blocks
    stacked = turned.reshape(2, blocks, SECOND, columns)
    twist_real = lax.dynamic_slice_in_dim(tables[2], block_start, blocks, 0)[..., None]
    twist_imag = lax.dynamic_slice_in_dim(tables[3], block_start, blocks, 0)[..., None]
    section_one = complex_times(
        contract("zkcx,wzbc->wkbx", stacked, tables[1]), twist_real, -twist_imag
    )
    section_one = section_one.astype(jnp.bfloat16)
    outer_count = patch_len // SECOND
    outer_ids = (offset_rows // SECOND + jnp.arange(outer_count, dtype=jnp.int32)) % FIRST
    patch_outer = jnp.take(tables[0][0], outer_ids, axis=1)
    phase_patch = contract(
        "zkbx,zak->abx", lax.all_gather(section_one, "dir", axis=1, tiled=True), patch_outer
    )
    phase_patch = phase_patch.reshape(patch_len, columns) * (1.0 / N)
    screen_field = propagate_columns(phase_patch, tables_y, slant_factor, fresnel_y)
    stacked_field = screen_field.reshape(2, row_count, ROWS_DEV, columns)
    portion = lax.all_to_all(stacked_field, "row", split_axis=1, concat_axis=3, tiled=True)
    item_count = portion.shape[2]
    stacked = portion.reshape(2, item_count, FIRST, SECOND)
    spectral = forward_axis(stacked, tables, fresnel_x, row_patterns, False)
    wave_field = inverse_axis(spectral, tables, row_patterns, False)
    intensity = wave_field[0] * wave_field[0] + wave_field[1] * wave_field[1]
    intensity = intensity.reshape(item_count, XTILES, TILE_X)
    tile_one = jnp.sum(intensity, axis=2)
    tile_two = jnp.sum(intensity * intensity, axis=2)
    tile_rows = ROWS_DEV // YTILES
    first_moment = jnp.sum(tile_one.reshape(YTILES, tile_rows, XTILES), axis=1)
    second_moment = jnp.sum(tile_two.reshape(YTILES, tile_rows, XTILES), axis=1)
    fluctuation, faded_power = tile_statistics(first_moment, second_moment, window[0], tile_rows)
    tile_total = faded_power.shape[0] * faded_power.shape[1]
    local_tile = tile_map[0] - lax.axis_index("row") * tile_total
    inside = (local_tile >= 0) & (local_tile < tile_total)
    tile_row = local_tile // XTILES
    tile_column = local_tile % XTILES
    pick_row = (tile_row[:, None] == jnp.arange(YTILES, dtype=jnp.int32)[None, :]).astype(jnp.float32)
    row_values = jnp.dot(pick_row, faded_power, precision=lax.Precision.HIGHEST)
    pick_column = tile_column[:, None] == jnp.arange(XTILES, dtype=jnp.int32)[None, :]
    looked = jnp.sum(jnp.where(pick_column, row_values, 0.0), axis=1)
    looked = jnp.where(inside, looked, 0.0)
    received = link_gain[0] * looked
    direction = lax.axis_index("dir")
    serves_here = serving == direction
    signal_part = jnp.where(serves_here, received, 0.0)
    interference_part = jnp.where(serves_here, 0.0, received)
    dir_count = lax.axis_size("dir")
    share_size = serving.shape[0] // (dir_count * row_count)
    parts = jnp.stack([signal_part, interference_part]).reshape(2, dir_count, row_count, share_size)
    parts = lax.all_to_all(parts, "row", split_axis=2, concat_axis=2, tiled=True)
    parts = jnp.sum(parts, axis=2, keepdims=True)
    parts = lax.all_to_all(parts, "dir", split_axis=1, concat_axis=1, tiled=True)
    parts = jnp.sum(parts, axis=(1, 2))
    signal, interference = parts[0], parts[1]
    signal_ratio = jnp.log10(signal / (interference + noise_floor))
    return (fluctuation[None], signal_ratio)


def solution(mesh):
    return jax.shard_map(
        body,
        mesh=mesh,
        in_specs=(
            P(None, ("dir", "row"), None),
            P("dir", None),
            P("dir"),
            P("dir", None),
            P("dir", None),
            P(),
        ),
        out_specs=(P("dir", "row", None), P(("dir", "row"))),
        check_vma=False,
    )
```

```python
import math

import jax
import jax.numpy as jnp
from jax import lax
from jax.sharding import PartitionSpec as P

N = 8192
FIRST = 64
SECOND = 128
ROWS_DEV = 32
XTILES = 128
YTILES = 8
TILE_X = 64


full_turn = 2.0 * math.pi
noise_floor = 0.05
tiny_value = 1e-06
strength = 1.6
row_patterns = (
    "zrab,zwak->wrkb",
    "zrkb,zwbc->wrkc",
    "zrkc,wzbc->wrkb",
    "zrkb,wzak->wrab",
    "zrkb,zak->rab",
)
column_patterns = (
    "zaby,zwak->wkby",
    "zkby,zwbc->wkcy",
    "zkcy,wzbc->wkby",
    "zkby,wzak->waby",
    "zkby,zak->aby",
)


def complex_block(real_part, imag_part):
    return jnp.stack(
        [jnp.stack([real_part, imag_part]), jnp.stack([-imag_part, real_part])]
    ).astype(jnp.bfloat16)


def transform_tables(first, second):
    total = first * second
    outer_ids = jnp.arange(first, dtype=jnp.int32)
    inner_ids = jnp.arange(second, dtype=jnp.int32)
    outer_angle = (outer_ids[:, None] * outer_ids[None, :] % first).astype(jnp.float32) * (
        full_turn / first
    )
    inner_angle = (inner_ids[:, None] * inner_ids[None, :] % second).astype(jnp.float32) * (
        full_turn / second
    )
    twist_angle = (outer_ids[:, None] * inner_ids[None, :] % total).astype(jnp.float32) * (
        full_turn / total
    )
    return (
        complex_block(jnp.cos(outer_angle), -jnp.sin(outer_angle)),
        complex_block(jnp.cos(inner_angle), -jnp.sin(inner_angle)),
        jnp.cos(twist_angle),
        -jnp.sin(twist_angle),
    )


def signed_wave(positions, first, second):
    total = first * second
    wave_number = positions // second + first * (positions % second)
    return jnp.where(wave_number >= total // 2, wave_number - total, wave_number).astype(
        jnp.float32
    )


def spectral_filter(row_ids, column_ids):
    wave_rows = signed_wave(row_ids, FIRST, SECOND)
    wave_columns = signed_wave(column_ids, FIRST, SECOND)
    squared_radius = 16.0 + wave_rows[:, None] ** 2 + wave_columns[None, :] ** 2
    return strength * float(N) * float(N) * squared_radius ** (-0.75)


def fresnel_factor(geometry_row, first, second):
    total = first * second
    fresnel_area = 144.0 * jnp.exp2(geometry_row[0].astype(jnp.float32))
    positions = jnp.arange(total, dtype=jnp.int32).reshape(first, second)
    scaled = signed_wave(positions, first, second) * (full_turn / total)
    turning = 0.5 * scaled * scaled * fresnel_area
    return (jnp.cos(turning), -jnp.sin(turning))


def complex_times(values, real_part, imag_part):
    return jnp.stack(
        [
            values[0] * real_part - values[1] * imag_part,
            values[0] * imag_part + values[1] * real_part,
        ]
    )


def contract(pattern, operand, matrix):
    return jnp.einsum(pattern, operand, matrix, preferred_element_type=jnp.float32)


def table_length(tables):
    return tables[0].shape[2] * tables[1].shape[2]


def forward_axis(values, tables, factor, patterns, trailing):
    outer_table, inner_table, twist_real, twist_imag = tables
    factor_real, factor_imag = factor
    if trailing:
        twist_real, twist_imag = (twist_real[..., None], twist_imag[..., None])
        factor_real, factor_imag = (factor_real[..., None], factor_imag[..., None])
    section_one = complex_times(
        contract(patterns[0], values, outer_table), twist_real, twist_imag
    ).astype(jnp.bfloat16)
    section_two = contract(patterns[1], section_one, inner_table)
    return complex_times(section_two, factor_real, factor_imag).astype(jnp.bfloat16)


def inverse_first(values, tables, patterns, trailing):
    outer_table, inner_table, twist_real, twist_imag = tables
    if trailing:
        twist_real, twist_imag = (twist_real[..., None], twist_imag[..., None])
    return complex_times(
        contract(patterns[2], values, inner_table), twist_real, -twist_imag
    ).astype(jnp.bfloat16)


def inverse_axis(values, tables, patterns, trailing):
    section_one = inverse_first(values, tables, patterns, trailing)
    return contract(patterns[3], section_one, tables[0]) * (1.0 / table_length(tables))


def window_matrix(half_width):
    positions = jnp.arange(XTILES, dtype=jnp.int32)
    difference = (positions[:, None] - positions[None, :]) % XTILES
    distance = jnp.minimum(difference, XTILES - difference)
    return (distance <= half_width).astype(jnp.float32)


def tile_statistics(first_moment, second_moment, half_width, tile_rows):
    window_mask = window_matrix(half_width)
    cells = ((2 * half_width + 1) * (TILE_X * tile_rows)).astype(jnp.float32)
    mean_one = jnp.dot(first_moment, window_mask, precision=lax.Precision.HIGHEST) / cells
    mean_two = jnp.dot(second_moment, window_mask, precision=lax.Precision.HIGHEST) / cells
    fluctuation = mean_two / (mean_one * mean_one + tiny_value) - 1.0
    return (fluctuation, mean_one * jnp.exp(-fluctuation))


def propagate_columns(phase_patch, tables_y, slant_factor, fresnel_y):
    patch_rows = phase_patch.shape[0]
    width_here = phase_patch.shape[1]
    outer_len = tables_y[0].shape[2]
    inner_len = tables_y[1].shape[2]
    turned_phase = slant_factor * phase_patch
    screen_field = jnp.stack([jnp.cos(turned_phase), jnp.sin(turned_phase)]).astype(jnp.bfloat16)
    stacked = screen_field.reshape(2, outer_len, inner_len, width_here)
    spectral = forward_axis(stacked, tables_y, fresnel_y, column_patterns, True)
    result = inverse_axis(spectral, tables_y, column_patterns, True)
    return result.astype(jnp.bfloat16).reshape(2, patch_rows, width_here)


def body(white_noise, geometry, window, tile_map, link_gain, serving):
    row_count = lax.axis_size("row")
    tables = transform_tables(FIRST, SECOND)
    tables_y = transform_tables(row_count, ROWS_DEV)
    patch_len = row_count * ROWS_DEV
    rows_here = white_noise.shape[1]
    row_start = lax.axis_index(("dir", "row")) * rows_here
    row_ids = row_start + jnp.arange(rows_here, dtype=jnp.int32)
    column_ids = jnp.arange(N, dtype=jnp.int32)
    spectral_gain = spectral_filter(row_ids, column_ids)
    spectrum = (white_noise.astype(jnp.float32) * spectral_gain).astype(jnp.bfloat16)
    section_first = inverse_first(
        spectrum.reshape(2, rows_here, FIRST, SECOND), tables, row_patterns, False
    )
    half_screen = contract("zrkb,wzak->awrb", section_first, tables[0]) * (1.0 / N)
    half_screen = half_screen.astype(jnp.bfloat16)
    turned = lax.all_to_all(half_screen, "row", split_axis=0, concat_axis=0, tiled=True)
    slant_factor = 1.0 + 0.25 * geometry[0, 1].astype(jnp.float32)
    fresnel_x = fresnel_factor(geometry[0], FIRST, SECOND)
    fresnel_y = fresnel_factor(geometry[0], row_count, ROWS_DEV)
    offset_rows = N // 4 * geometry[0, 1]
    columns = SECOND
    blocks = row_count * rows_here // SECOND
    split = SECOND // rows_here
    block_start = lax.axis_index("dir") * blocks
    stacked = turned.reshape(blocks, split, 2, rows_here, columns)
    inner_split = tables[1].reshape(2, 2, SECOND, split, rows_here)
    twist_real = lax.dynamic_slice_in_dim(tables[2], block_start, blocks, 0)[..., None]
    twist_imag = lax.dynamic_slice_in_dim(tables[3], block_start, blocks, 0)[..., None]
    section_one = complex_times(
        contract("khzrx,wzbhr->wkbx", stacked, inner_split), twist_real, -twist_imag
    )
    section_one = section_one.astype(jnp.bfloat16)
    outer_count = patch_len // SECOND
    outer_ids = (offset_rows // SECOND + jnp.arange(outer_count, dtype=jnp.int32)) % FIRST
    patch_outer = jnp.take(tables[0][0], outer_ids, axis=1)
    phase_patch = contract(
        "zkbx,zak->abx", lax.all_gather(section_one, "dir", axis=1, tiled=True), patch_outer
    )
    phase_patch = phase_patch.reshape(patch_len, columns) * (1.0 / N)
    screen_field = propagate_columns(phase_patch, tables_y, slant_factor, fresnel_y)
    stacked_field = screen_field.reshape(2, row_count, ROWS_DEV, columns)
    portion = lax.all_to_all(stacked_field, "row", split_axis=1, concat_axis=3, tiled=True)
    item_count = portion.shape[2]
    stacked = portion.reshape(2, item_count, FIRST, SECOND)
    spectral = forward_axis(stacked, tables, fresnel_x, row_patterns, False)
    wave_field = inverse_axis(spectral, tables, row_patterns, False)
    intensity = wave_field[0] * wave_field[0] + wave_field[1] * wave_field[1]
    intensity = intensity.reshape(item_count, XTILES, TILE_X)
    tile_one = jnp.sum(intensity, axis=2)
    tile_two = jnp.sum(intensity * intensity, axis=2)
    tile_rows = ROWS_DEV // YTILES
    first_moment = jnp.sum(tile_one.reshape(YTILES, tile_rows, XTILES), axis=1)
    second_moment = jnp.sum(tile_two.reshape(YTILES, tile_rows, XTILES), axis=1)
    fluctuation, faded_power = tile_statistics(first_moment, second_moment, window[0], tile_rows)
    tile_total = faded_power.shape[0] * faded_power.shape[1]
    local_tile = tile_map[0] - lax.axis_index("row") * tile_total
    inside = (local_tile >= 0) & (local_tile < tile_total)
    tile_row = local_tile // XTILES
    tile_column = local_tile % XTILES
    pick_row = (tile_row[:, None] == jnp.arange(YTILES, dtype=jnp.int32)[None, :]).astype(jnp.float32)
    row_values = jnp.dot(pick_row, faded_power, precision=lax.Precision.HIGHEST)
    pick_column = tile_column[:, None] == jnp.arange(XTILES, dtype=jnp.int32)[None, :]
    looked = jnp.sum(jnp.where(pick_column, row_values, 0.0), axis=1)
    looked = jnp.where(inside, looked, 0.0)
    received = link_gain[0] * looked
    direction = lax.axis_index("dir")
    serves_here = serving == direction
    signal_part = jnp.where(serves_here, received, 0.0)
    interference_part = jnp.where(serves_here, 0.0, received)
    dir_count = lax.axis_size("dir")
    share_size = serving.shape[0] // (dir_count * row_count)
    parts = jnp.stack([signal_part, interference_part]).reshape(2, dir_count, row_count, share_size)
    parts = lax.all_to_all(parts, "row", split_axis=2, concat_axis=2, tiled=True)
    parts = jnp.sum(parts, axis=2, keepdims=True)
    parts = lax.all_to_all(parts, "dir", split_axis=1, concat_axis=1, tiled=True)
    parts = jnp.sum(parts, axis=(1, 2))
    signal, interference = parts[0], parts[1]
    signal_ratio = jnp.log10(signal / (interference + noise_floor))
    return (fluctuation[None], signal_ratio)


def solution(mesh):
    return jax.shard_map(
        body,
        mesh=mesh,
        in_specs=(
            P(None, ("dir", "row"), None),
            P("dir", None),
            P("dir"),
            P("dir", None),
            P("dir", None),
            P(),
        ),
        out_specs=(P("dir", "row", None), P(("dir", "row"))),
        check_vma=False,
    )
```

```python
import math

import jax
import jax.numpy as jnp
from jax import lax
from jax.sharding import PartitionSpec as P

N = 8192
FIRST = 64
SECOND = 128
ROWS_DEV = 32
XTILES = 128
YTILES = 8
TILE_X = 64


full_turn = 2.0 * math.pi
noise_floor = 0.05
tiny_value = 1e-06
strength = 1.6
row_patterns = (
    "zrab,zwak->wrkb",
    "zrkb,zwbc->wrkc",
    "zrkc,wzbc->wrkb",
    "zrkb,wzak->wrab",
    "zrkb,zak->rab",
)
column_patterns = (
    "zaby,zwak->wkby",
    "zkby,zwbc->wkcy",
    "zkcy,wzbc->wkby",
    "zkby,wzak->waby",
    "zkby,zak->aby",
)


def complex_block(real_part, imag_part):
    return jnp.stack(
        [jnp.stack([real_part, imag_part]), jnp.stack([-imag_part, real_part])]
    ).astype(jnp.bfloat16)


def transform_tables(first, second):
    total = first * second
    outer_ids = jnp.arange(first, dtype=jnp.int32)
    inner_ids = jnp.arange(second, dtype=jnp.int32)
    outer_angle = (outer_ids[:, None] * outer_ids[None, :] % first).astype(jnp.float32) * (
        full_turn / first
    )
    inner_angle = (inner_ids[:, None] * inner_ids[None, :] % second).astype(jnp.float32) * (
        full_turn / second
    )
    twist_angle = (outer_ids[:, None] * inner_ids[None, :] % total).astype(jnp.float32) * (
        full_turn / total
    )
    return (
        complex_block(jnp.cos(outer_angle), -jnp.sin(outer_angle)),
        complex_block(jnp.cos(inner_angle), -jnp.sin(inner_angle)),
        jnp.cos(twist_angle),
        -jnp.sin(twist_angle),
    )


def signed_wave(positions, first, second):
    total = first * second
    wave_number = positions // second + first * (positions % second)
    return jnp.where(wave_number >= total // 2, wave_number - total, wave_number).astype(
        jnp.float32
    )


def spectral_filter(row_ids, column_ids):
    wave_rows = signed_wave(row_ids, FIRST, SECOND)
    wave_columns = signed_wave(column_ids, FIRST, SECOND)
    squared_radius = 16.0 + wave_rows[:, None] ** 2 + wave_columns[None, :] ** 2
    return strength * float(N) * float(N) * squared_radius ** (-0.75)


def fresnel_factor(geometry_row, first, second):
    total = first * second
    fresnel_area = 144.0 * jnp.exp2(geometry_row[0].astype(jnp.float32))
    positions = jnp.arange(total, dtype=jnp.int32).reshape(first, second)
    scaled = signed_wave(positions, first, second) * (full_turn / total)
    turning = 0.5 * scaled * scaled * fresnel_area
    return (jnp.cos(turning), -jnp.sin(turning))


def complex_times(values, real_part, imag_part):
    return jnp.stack(
        [
            values[0] * real_part - values[1] * imag_part,
            values[0] * imag_part + values[1] * real_part,
        ]
    )


def contract(pattern, operand, matrix):
    return jnp.einsum(pattern, operand, matrix, preferred_element_type=jnp.float32)


def table_length(tables):
    return tables[0].shape[2] * tables[1].shape[2]


def forward_axis(values, tables, factor, patterns, trailing):
    outer_table, inner_table, twist_real, twist_imag = tables
    factor_real, factor_imag = factor
    if trailing:
        twist_real, twist_imag = (twist_real[..., None], twist_imag[..., None])
        factor_real, factor_imag = (factor_real[..., None], factor_imag[..., None])
    section_one = complex_times(
        contract(patterns[0], values, outer_table), twist_real, twist_imag
    ).astype(jnp.bfloat16)
    section_two = contract(patterns[1], section_one, inner_table)
    return complex_times(section_two, factor_real, factor_imag).astype(jnp.bfloat16)


def inverse_first(values, tables, patterns, trailing):
    outer_table, inner_table, twist_real, twist_imag = tables
    if trailing:
        twist_real, twist_imag = (twist_real[..., None], twist_imag[..., None])
    return complex_times(
        contract(patterns[2], values, inner_table), twist_real, -twist_imag
    ).astype(jnp.bfloat16)


def inverse_axis(values, tables, patterns, trailing):
    section_one = inverse_first(values, tables, patterns, trailing)
    return contract(patterns[3], section_one, tables[0]) * (1.0 / table_length(tables))


def window_matrix(half_width):
    positions = jnp.arange(XTILES, dtype=jnp.int32)
    difference = (positions[:, None] - positions[None, :]) % XTILES
    distance = jnp.minimum(difference, XTILES - difference)
    return (distance <= half_width).astype(jnp.float32)


def tile_statistics(first_moment, second_moment, half_width, tile_rows):
    window_mask = window_matrix(half_width)
    cells = ((2 * half_width + 1) * (TILE_X * tile_rows)).astype(jnp.float32)
    mean_one = jnp.dot(first_moment, window_mask, precision=lax.Precision.HIGHEST) / cells
    mean_two = jnp.dot(second_moment, window_mask, precision=lax.Precision.HIGHEST) / cells
    fluctuation = mean_two / (mean_one * mean_one + tiny_value) - 1.0
    return (fluctuation, mean_one * jnp.exp(-fluctuation))


def propagate_columns(phase_patch, tables_y, slant_factor, fresnel_y):
    patch_rows = phase_patch.shape[0]
    width_here = phase_patch.shape[1]
    outer_len = tables_y[0].shape[2]
    inner_len = tables_y[1].shape[2]
    turned_phase = slant_factor * phase_patch
    screen_field = jnp.stack([jnp.cos(turned_phase), jnp.sin(turned_phase)]).astype(jnp.bfloat16)
    stacked = screen_field.reshape(2, outer_len, inner_len, width_here)
    spectral = forward_axis(stacked, tables_y, fresnel_y, column_patterns, True)
    result = inverse_axis(spectral, tables_y, column_patterns, True)
    return result.astype(jnp.bfloat16).reshape(2, patch_rows, width_here)


def column_front(chunk, tables, row_count, rows_here):
    turned = lax.all_to_all(chunk, "row", split_axis=0, concat_axis=0, tiled=True)
    columns = chunk.shape[-1]
    blocks = row_count * rows_here // SECOND
    split = SECOND // rows_here
    block_start = lax.axis_index("dir") * blocks
    stacked = turned.reshape(blocks, split, 2, rows_here, columns)
    inner_split = tables[1].reshape(2, 2, SECOND, split, rows_here)
    twist_real = lax.dynamic_slice_in_dim(tables[2], block_start, blocks, 0)[..., None]
    twist_imag = lax.dynamic_slice_in_dim(tables[3], block_start, blocks, 0)[..., None]
    section_one = complex_times(
        contract("khzrx,wzbhr->wkbx", stacked, inner_split), twist_real, -twist_imag
    )
    return section_one.astype(jnp.bfloat16)


def column_tail(gathered, tables, tables_y, slant_factor, fresnel_y, offset_rows, patch_len, row_count):
    columns = gathered.shape[-1]
    outer_count = patch_len // SECOND
    outer_ids = (offset_rows // SECOND + jnp.arange(outer_count, dtype=jnp.int32)) % FIRST
    patch_outer = jnp.take(tables[0][0], outer_ids, axis=1)
    phase_patch = contract("zkbx,zak->abx", gathered, patch_outer)
    phase_patch = phase_patch.reshape(patch_len, columns) * (1.0 / N)
    screen_field = propagate_columns(phase_patch, tables_y, slant_factor, fresnel_y)
    stacked_field = screen_field.reshape(2, row_count, ROWS_DEV, columns)
    return lax.all_to_all(stacked_field, "row", split_axis=1, concat_axis=3, tiled=True)


def body(white_noise, geometry, window, tile_map, link_gain, serving):
    row_count = lax.axis_size("row")
    tables = transform_tables(FIRST, SECOND)
    tables_y = transform_tables(row_count, ROWS_DEV)
    patch_len = row_count * ROWS_DEV
    rows_here = white_noise.shape[1]
    row_start = lax.axis_index(("dir", "row")) * rows_here
    row_ids = row_start + jnp.arange(rows_here, dtype=jnp.int32)
    column_ids = jnp.arange(N, dtype=jnp.int32)
    spectral_gain = spectral_filter(row_ids, column_ids)
    spectrum = (white_noise.astype(jnp.float32) * spectral_gain).astype(jnp.bfloat16)
    section_first = inverse_first(
        spectrum.reshape(2, rows_here, FIRST, SECOND), tables, row_patterns, False
    )
    half_screen = contract("zrkb,wzak->awrb", section_first, tables[0]) * (1.0 / N)
    half_screen = half_screen.astype(jnp.bfloat16)
    slant_factor = 1.0 + 0.25 * geometry[0, 1].astype(jnp.float32)
    fresnel_x = fresnel_factor(geometry[0], FIRST, SECOND)
    fresnel_y = fresnel_factor(geometry[0], row_count, ROWS_DEV)
    offset_rows = N // 4 * geometry[0, 1]
    pieces = 2
    piece_width = SECOND // pieces
    portions = []
    previous = None
    for piece in range(pieces):
        chunk = half_screen[..., piece * piece_width : (piece + 1) * piece_width]
        if previous is not None:
            previous, chunk = lax.optimization_barrier((previous, chunk))
        section_one = column_front(chunk, tables, row_count, rows_here)
        gathered = lax.all_gather(section_one, "dir", axis=1, tiled=True)
        if portions:
            portions[-1], gathered = lax.optimization_barrier((portions[-1], gathered))
        portions.append(
            column_tail(
                gathered, tables, tables_y, slant_factor, fresnel_y, offset_rows, patch_len, row_count
            )
        )
        previous = section_one
    portion = jnp.stack(
        [p.reshape(2, ROWS_DEV, row_count, piece_width) for p in portions], axis=3
    ).reshape(2, 1, ROWS_DEV, N)
    item_count = portion.shape[2]
    stacked = portion.reshape(2, item_count, FIRST, SECOND)
    spectral = forward_axis(stacked, tables, fresnel_x, row_patterns, False)
    wave_field = inverse_axis(spectral, tables, row_patterns, False)
    intensity = wave_field[0] * wave_field[0] + wave_field[1] * wave_field[1]
    intensity = intensity.reshape(item_count, XTILES, TILE_X)
    tile_one = jnp.sum(intensity, axis=2)
    tile_two = jnp.sum(intensity * intensity, axis=2)
    tile_rows = ROWS_DEV // YTILES
    first_moment = jnp.sum(tile_one.reshape(YTILES, tile_rows, XTILES), axis=1)
    second_moment = jnp.sum(tile_two.reshape(YTILES, tile_rows, XTILES), axis=1)
    fluctuation, faded_power = tile_statistics(first_moment, second_moment, window[0], tile_rows)
    tile_total = faded_power.shape[0] * faded_power.shape[1]
    local_tile = tile_map[0] - lax.axis_index("row") * tile_total
    inside = (local_tile >= 0) & (local_tile < tile_total)
    tile_row = local_tile // XTILES
    tile_column = local_tile % XTILES
    pick_row = (tile_row[:, None] == jnp.arange(YTILES, dtype=jnp.int32)[None, :]).astype(jnp.float32)
    row_values = jnp.dot(pick_row, faded_power, precision=lax.Precision.HIGHEST)
    pick_column = tile_column[:, None] == jnp.arange(XTILES, dtype=jnp.int32)[None, :]
    looked = jnp.sum(jnp.where(pick_column, row_values, 0.0), axis=1)
    looked = jnp.where(inside, looked, 0.0)
    received = link_gain[0] * looked
    direction = lax.axis_index("dir")
    serves_here = serving == direction
    signal_part = jnp.where(serves_here, received, 0.0)
    interference_part = jnp.where(serves_here, 0.0, received)
    dir_count = lax.axis_size("dir")
    share_size = serving.shape[0] // (dir_count * row_count)
    parts = jnp.stack([signal_part, interference_part]).reshape(2, dir_count, row_count, share_size)
    parts = lax.all_to_all(parts, "row", split_axis=2, concat_axis=2, tiled=True)
    parts = jnp.sum(parts, axis=2, keepdims=True)
    parts = lax.all_to_all(parts, "dir", split_axis=1, concat_axis=1, tiled=True)
    parts = jnp.sum(parts, axis=(1, 2))
    signal, interference = parts[0], parts[1]
    signal_ratio = jnp.log10(signal / (interference + noise_floor))
    return (fluctuation[None], signal_ratio)


def solution(mesh):
    return jax.shard_map(
        body,
        mesh=mesh,
        in_specs=(
            P(None, ("dir", "row"), None),
            P("dir", None),
            P("dir"),
            P("dir", None),
            P("dir", None),
            P(),
        ),
        out_specs=(P("dir", "row", None), P(("dir", "row"))),
        check_vma=False,
    )
```

```python
import math

import jax
import jax.numpy as jnp
from jax import lax
from jax.sharding import PartitionSpec as P

N = 8192
FIRST = 64
SECOND = 128
ROWS_DEV = 32
XTILES = 128
YTILES = 8
TILE_X = 64


full_turn = 2.0 * math.pi
noise_floor = 0.05
tiny_value = 1e-06
strength = 1.6
row_patterns = (
    "zrab,zwak->wrkb",
    "zrkb,zwbc->wrkc",
    "zrkc,wzbc->wrkb",
    "zrkb,wzak->wrab",
    "zrkb,zak->rab",
)
column_patterns = (
    "zaby,zwak->wkby",
    "zkby,zwbc->wkcy",
    "zkcy,wzbc->wkby",
    "zkby,wzak->waby",
    "zkby,zak->aby",
)


def complex_block(real_part, imag_part):
    return jnp.stack(
        [jnp.stack([real_part, imag_part]), jnp.stack([-imag_part, real_part])]
    ).astype(jnp.bfloat16)


def transform_tables(first, second):
    total = first * second
    outer_ids = jnp.arange(first, dtype=jnp.int32)
    inner_ids = jnp.arange(second, dtype=jnp.int32)
    outer_angle = (outer_ids[:, None] * outer_ids[None, :] % first).astype(jnp.float32) * (
        full_turn / first
    )
    inner_angle = (inner_ids[:, None] * inner_ids[None, :] % second).astype(jnp.float32) * (
        full_turn / second
    )
    twist_angle = (outer_ids[:, None] * inner_ids[None, :] % total).astype(jnp.float32) * (
        full_turn / total
    )
    return (
        complex_block(jnp.cos(outer_angle), -jnp.sin(outer_angle)),
        complex_block(jnp.cos(inner_angle), -jnp.sin(inner_angle)),
        jnp.cos(twist_angle),
        -jnp.sin(twist_angle),
    )


def signed_wave(positions, first, second):
    total = first * second
    wave_number = positions // second + first * (positions % second)
    return jnp.where(wave_number >= total // 2, wave_number - total, wave_number).astype(
        jnp.float32
    )


def spectral_filter(row_ids, column_ids):
    wave_rows = signed_wave(row_ids, FIRST, SECOND)
    wave_columns = signed_wave(column_ids, FIRST, SECOND)
    squared_radius = 16.0 + wave_rows[:, None] ** 2 + wave_columns[None, :] ** 2
    return strength * float(N) * float(N) * squared_radius ** (-0.75)


def fresnel_factor(geometry_row, first, second):
    total = first * second
    fresnel_area = 144.0 * jnp.exp2(geometry_row[0].astype(jnp.float32))
    positions = jnp.arange(total, dtype=jnp.int32).reshape(first, second)
    scaled = signed_wave(positions, first, second) * (full_turn / total)
    turning = 0.5 * scaled * scaled * fresnel_area
    return (jnp.cos(turning), -jnp.sin(turning))


def complex_times(values, real_part, imag_part):
    return jnp.stack(
        [
            values[0] * real_part - values[1] * imag_part,
            values[0] * imag_part + values[1] * real_part,
        ]
    )


def contract(pattern, operand, matrix):
    return jnp.einsum(pattern, operand, matrix, preferred_element_type=jnp.float32)


def table_length(tables):
    return tables[0].shape[2] * tables[1].shape[2]


def forward_axis(values, tables, factor, patterns, trailing):
    outer_table, inner_table, twist_real, twist_imag = tables
    factor_real, factor_imag = factor
    if trailing:
        twist_real, twist_imag = (twist_real[..., None], twist_imag[..., None])
        factor_real, factor_imag = (factor_real[..., None], factor_imag[..., None])
    section_one = complex_times(
        contract(patterns[0], values, outer_table), twist_real, twist_imag
    ).astype(jnp.bfloat16)
    section_two = contract(patterns[1], section_one, inner_table)
    return complex_times(section_two, factor_real, factor_imag).astype(jnp.bfloat16)


def inverse_first(values, tables, patterns, trailing):
    outer_table, inner_table, twist_real, twist_imag = tables
    if trailing:
        twist_real, twist_imag = (twist_real[..., None], twist_imag[..., None])
    return complex_times(
        contract(patterns[2], values, inner_table), twist_real, -twist_imag
    ).astype(jnp.bfloat16)


def inverse_axis(values, tables, patterns, trailing):
    section_one = inverse_first(values, tables, patterns, trailing)
    return contract(patterns[3], section_one, tables[0]) * (1.0 / table_length(tables))


def window_matrix(half_width):
    positions = jnp.arange(XTILES, dtype=jnp.int32)
    difference = (positions[:, None] - positions[None, :]) % XTILES
    distance = jnp.minimum(difference, XTILES - difference)
    return (distance <= half_width).astype(jnp.float32)


def tile_statistics(first_moment, second_moment, half_width, tile_rows):
    window_mask = window_matrix(half_width)
    cells = ((2 * half_width + 1) * (TILE_X * tile_rows)).astype(jnp.float32)
    mean_one = jnp.dot(first_moment, window_mask, precision=lax.Precision.HIGHEST) / cells
    mean_two = jnp.dot(second_moment, window_mask, precision=lax.Precision.HIGHEST) / cells
    fluctuation = mean_two / (mean_one * mean_one + tiny_value) - 1.0
    return (fluctuation, mean_one * jnp.exp(-fluctuation))


def propagate_columns(phase_patch, tables_y, slant_factor, fresnel_y):
    patch_rows = phase_patch.shape[0]
    width_here = phase_patch.shape[1]
    outer_len = tables_y[0].shape[2]
    inner_len = tables_y[1].shape[2]
    turned_phase = slant_factor * phase_patch
    screen_field = jnp.stack([jnp.cos(turned_phase), jnp.sin(turned_phase)]).astype(jnp.bfloat16)
    stacked = screen_field.reshape(2, outer_len, inner_len, width_here)
    spectral = forward_axis(stacked, tables_y, fresnel_y, column_patterns, True)
    result = inverse_axis(spectral, tables_y, column_patterns, True)
    return result.astype(jnp.bfloat16).reshape(2, patch_rows, width_here)


def body(white_noise, geometry, window, tile_map, link_gain, serving):
    row_count = lax.axis_size("row")
    tables = transform_tables(FIRST, SECOND)
    tables_y = transform_tables(row_count, ROWS_DEV)
    patch_len = row_count * ROWS_DEV
    rows_here = white_noise.shape[1]
    row_start = lax.axis_index(("dir", "row")) * rows_here
    row_ids = row_start + jnp.arange(rows_here, dtype=jnp.int32)
    column_ids = jnp.arange(N, dtype=jnp.int32)
    spectral_gain = spectral_filter(row_ids, column_ids)
    spectrum = (white_noise.astype(jnp.float32) * spectral_gain).astype(jnp.bfloat16)
    section_first = inverse_first(
        spectrum.reshape(2, rows_here, FIRST, SECOND), tables, row_patterns, False
    )
    half_screen = contract("zrkb,wzak->awrb", section_first, tables[0]) * (1.0 / N)
    half_screen = half_screen.astype(jnp.bfloat16)
    turned = lax.all_to_all(half_screen, "row", split_axis=0, concat_axis=0, tiled=True)
    slant_factor = 1.0 + 0.25 * geometry[0, 1].astype(jnp.float32)
    fresnel_x = fresnel_factor(geometry[0], FIRST, SECOND)
    fresnel_y = fresnel_factor(geometry[0], row_count, ROWS_DEV)
    offset_rows = N // 4 * geometry[0, 1]
    columns = SECOND
    blocks = row_count * rows_here // SECOND
    split = SECOND // rows_here
    block_start = lax.axis_index("dir") * blocks
    stacked = turned.reshape(blocks, split, 2, rows_here, columns)
    inner_split = tables[1].reshape(2, 2, SECOND, split, rows_here)
    twist_real = lax.dynamic_slice_in_dim(tables[2], block_start, blocks, 0)[..., None]
    twist_imag = lax.dynamic_slice_in_dim(tables[3], block_start, blocks, 0)[..., None]
    section_one = complex_times(
        contract("khzrx,wzbhr->wkbx", stacked, inner_split), twist_real, -twist_imag
    )
    section_one = jnp.transpose(section_one.astype(jnp.bfloat16), (1, 0, 2, 3))
    outer_count = patch_len // SECOND
    outer_ids = (offset_rows // SECOND + jnp.arange(outer_count, dtype=jnp.int32)) % FIRST
    patch_outer = jnp.take(tables[0][0], outer_ids, axis=1)
    phase_patch = contract(
        "kzbx,zak->abx", lax.all_gather(section_one, "dir", axis=0, tiled=True), patch_outer
    )
    phase_patch = phase_patch.reshape(patch_len, columns) * (1.0 / N)
    screen_field = propagate_columns(phase_patch, tables_y, slant_factor, fresnel_y)
    stacked_field = jnp.transpose(screen_field.reshape(2, row_count, ROWS_DEV, columns), (1, 0, 2, 3))
    portion = lax.all_to_all(stacked_field, "row", split_axis=0, concat_axis=0, tiled=True)
    item_count = portion.shape[2]
    spectral = forward_axis(portion, tables, fresnel_x, ("azrb,zwak->wrkb",) + row_patterns[1:], False)
    wave_field = inverse_axis(spectral, tables, row_patterns, False)
    intensity = wave_field[0] * wave_field[0] + wave_field[1] * wave_field[1]
    intensity = intensity.reshape(item_count, XTILES, TILE_X)
    tile_one = jnp.sum(intensity, axis=2)
    tile_two = jnp.sum(intensity * intensity, axis=2)
    tile_rows = ROWS_DEV // YTILES
    first_moment = jnp.sum(tile_one.reshape(YTILES, tile_rows, XTILES), axis=1)
    second_moment = jnp.sum(tile_two.reshape(YTILES, tile_rows, XTILES), axis=1)
    fluctuation, faded_power = tile_statistics(first_moment, second_moment, window[0], tile_rows)
    tile_total = faded_power.shape[0] * faded_power.shape[1]
    local_tile = tile_map[0] - lax.axis_index("row") * tile_total
    inside = (local_tile >= 0) & (local_tile < tile_total)
    tile_row = local_tile // XTILES
    tile_column = local_tile % XTILES
    pick_row = (tile_row[:, None] == jnp.arange(YTILES, dtype=jnp.int32)[None, :]).astype(jnp.float32)
    row_values = jnp.dot(pick_row, faded_power, precision=lax.Precision.HIGHEST)
    pick_column = tile_column[:, None] == jnp.arange(XTILES, dtype=jnp.int32)[None, :]
    looked = jnp.sum(jnp.where(pick_column, row_values, 0.0), axis=1)
    looked = jnp.where(inside, looked, 0.0)
    received = link_gain[0] * looked
    direction = lax.axis_index("dir")
    serves_here = serving == direction
    signal_part = jnp.where(serves_here, received, 0.0)
    interference_part = jnp.where(serves_here, 0.0, received)
    dir_count = lax.axis_size("dir")
    share_size = serving.shape[0] // (dir_count * row_count)
    parts = jnp.stack([signal_part, interference_part]).reshape(2, dir_count, row_count, share_size)
    parts = lax.all_to_all(parts, "row", split_axis=2, concat_axis=2, tiled=True)
    parts = jnp.sum(parts, axis=2, keepdims=True)
    parts = lax.all_to_all(parts, "dir", split_axis=1, concat_axis=1, tiled=True)
    parts = jnp.sum(parts, axis=(1, 2))
    signal, interference = parts[0], parts[1]
    signal_ratio = jnp.log10(signal / (interference + noise_floor))
    return (fluctuation[None], signal_ratio)


def solution(mesh):
    return jax.shard_map(
        body,
        mesh=mesh,
        in_specs=(
            P(None, ("dir", "row"), None),
            P("dir", None),
            P("dir"),
            P("dir", None),
            P("dir", None),
            P(),
        ),
        out_specs=(P("dir", "row", None), P(("dir", "row"))),
        check_vma=False,
    )
```

```python
import math

import jax
import jax.numpy as jnp
from jax import lax
from jax.sharding import PartitionSpec as P

N = 8192
FIRST = 64
SECOND = 128
ROWS_DEV = 32
XTILES = 128
YTILES = 8
TILE_X = 64


full_turn = 2.0 * math.pi
noise_floor = 0.05
tiny_value = 1e-06
strength = 1.6
row_patterns = (
    "zrab,zwak->wrkb",
    "zrkb,zwbc->wrkc",
    "zrkc,wzbc->wrkb",
    "zrkb,wzak->wrab",
    "zrkb,zak->rab",
)
column_patterns = (
    "zaby,zwak->wkby",
    "zkby,zwbc->wkcy",
    "zkcy,wzbc->wkby",
    "zkby,wzak->waby",
    "zkby,zak->aby",
)


def complex_block(real_part, imag_part):
    return jnp.stack(
        [jnp.stack([real_part, imag_part]), jnp.stack([-imag_part, real_part])]
    ).astype(jnp.bfloat16)


def transform_tables(first, second):
    total = first * second
    outer_ids = jnp.arange(first, dtype=jnp.int32)
    inner_ids = jnp.arange(second, dtype=jnp.int32)
    outer_angle = (outer_ids[:, None] * outer_ids[None, :] % first).astype(jnp.float32) * (
        full_turn / first
    )
    inner_angle = (inner_ids[:, None] * inner_ids[None, :] % second).astype(jnp.float32) * (
        full_turn / second
    )
    twist_angle = (outer_ids[:, None] * inner_ids[None, :] % total).astype(jnp.float32) * (
        full_turn / total
    )
    return (
        complex_block(jnp.cos(outer_angle), -jnp.sin(outer_angle)),
        complex_block(jnp.cos(inner_angle), -jnp.sin(inner_angle)),
        jnp.cos(twist_angle),
        -jnp.sin(twist_angle),
    )


def signed_wave(positions, first, second):
    total = first * second
    wave_number = positions // second + first * (positions % second)
    return jnp.where(wave_number >= total // 2, wave_number - total, wave_number).astype(
        jnp.float32
    )


def spectral_filter(row_ids, column_ids):
    wave_rows = signed_wave(row_ids, FIRST, SECOND)
    wave_columns = signed_wave(column_ids, FIRST, SECOND)
    squared_radius = 16.0 + wave_rows[:, None] ** 2 + wave_columns[None, :] ** 2
    return strength * float(N) * float(N) * squared_radius ** (-0.75)


def fresnel_factor(geometry_row, first, second):
    total = first * second
    fresnel_area = 144.0 * jnp.exp2(geometry_row[0].astype(jnp.float32))
    positions = jnp.arange(total, dtype=jnp.int32).reshape(first, second)
    scaled = signed_wave(positions, first, second) * (full_turn / total)
    turning = 0.5 * scaled * scaled * fresnel_area
    return (jnp.cos(turning), -jnp.sin(turning))


def complex_times(values, real_part, imag_part):
    return jnp.stack(
        [
            values[0] * real_part - values[1] * imag_part,
            values[0] * imag_part + values[1] * real_part,
        ]
    )


def contract(pattern, operand, matrix):
    return jnp.einsum(pattern, operand, matrix, preferred_element_type=jnp.float32)


def table_length(tables):
    return tables[0].shape[2] * tables[1].shape[2]


def forward_axis(values, tables, factor, patterns, trailing):
    outer_table, inner_table, twist_real, twist_imag = tables
    factor_real, factor_imag = factor
    if trailing:
        twist_real, twist_imag = (twist_real[..., None], twist_imag[..., None])
        factor_real, factor_imag = (factor_real[..., None], factor_imag[..., None])
    section_one = complex_times(
        contract(patterns[0], values, outer_table), twist_real, twist_imag
    ).astype(jnp.bfloat16)
    section_two = contract(patterns[1], section_one, inner_table)
    return complex_times(section_two, factor_real, factor_imag).astype(jnp.bfloat16)


def inverse_first(values, tables, patterns, trailing):
    outer_table, inner_table, twist_real, twist_imag = tables
    if trailing:
        twist_real, twist_imag = (twist_real[..., None], twist_imag[..., None])
    return complex_times(
        contract(patterns[2], values, inner_table), twist_real, -twist_imag
    ).astype(jnp.bfloat16)


def inverse_axis(values, tables, patterns, trailing):
    section_one = inverse_first(values, tables, patterns, trailing)
    return contract(patterns[3], section_one, tables[0]) * (1.0 / table_length(tables))


def window_matrix(half_width):
    positions = jnp.arange(XTILES, dtype=jnp.int32)
    difference = (positions[:, None] - positions[None, :]) % XTILES
    distance = jnp.minimum(difference, XTILES - difference)
    return (distance <= half_width).astype(jnp.float32)


def tile_statistics(first_moment, second_moment, half_width, tile_rows):
    window_mask = window_matrix(half_width)
    cells = ((2 * half_width + 1) * (TILE_X * tile_rows)).astype(jnp.float32)
    mean_one = jnp.dot(first_moment, window_mask, precision=lax.Precision.HIGHEST) / cells
    mean_two = jnp.dot(second_moment, window_mask, precision=lax.Precision.HIGHEST) / cells
    fluctuation = mean_two / (mean_one * mean_one + tiny_value) - 1.0
    return (fluctuation, mean_one * jnp.exp(-fluctuation))


def propagate_columns(phase_patch, tables_y, slant_factor, fresnel_y):
    patch_rows = phase_patch.shape[0]
    width_here = phase_patch.shape[1]
    outer_len = tables_y[0].shape[2]
    inner_len = tables_y[1].shape[2]
    turned_phase = slant_factor * phase_patch
    screen_field = jnp.stack([jnp.cos(turned_phase), jnp.sin(turned_phase)]).astype(jnp.bfloat16)
    stacked = screen_field.reshape(2, outer_len, inner_len, width_here)
    spectral = forward_axis(stacked, tables_y, fresnel_y, column_patterns, True)
    result = inverse_axis(spectral, tables_y, column_patterns, True)
    return result.astype(jnp.bfloat16).reshape(2, patch_rows, width_here)


def body(white_noise, geometry, window, tile_map, link_gain, serving):
    row_count = lax.axis_size("row")
    tables = transform_tables(FIRST, SECOND)
    tables_y = transform_tables(row_count, ROWS_DEV)
    patch_len = row_count * ROWS_DEV
    rows_here = white_noise.shape[1]
    row_start = lax.axis_index(("dir", "row")) * rows_here
    row_ids = row_start + jnp.arange(rows_here, dtype=jnp.int32)
    column_ids = jnp.arange(N, dtype=jnp.int32)
    spectral_gain = spectral_filter(row_ids, column_ids)
    spectrum = (white_noise.astype(jnp.float32) * spectral_gain).astype(jnp.bfloat16)
    section_first = inverse_first(
        spectrum.reshape(2, rows_here, FIRST, SECOND), tables, row_patterns, False
    )
    half_screen = contract("zrkb,wzak->awrb", section_first, tables[0]) * (1.0 / N)
    half_screen = half_screen.astype(jnp.bfloat16)
    turned = lax.all_to_all(half_screen, "row", split_axis=0, concat_axis=0, tiled=True)
    slant_factor = 1.0 + 0.25 * geometry[0, 1].astype(jnp.float32)
    fresnel_x = fresnel_factor(geometry[0], FIRST, SECOND)
    fresnel_y = fresnel_factor(geometry[0], row_count, ROWS_DEV)
    offset_rows = N // 4 * geometry[0, 1]
    columns = SECOND
    blocks = row_count * rows_here // SECOND
    split = SECOND // rows_here
    block_start = lax.axis_index("dir") * blocks
    stacked = turned.reshape(blocks, split, 2, rows_here, columns)
    inner_split = tables[1].reshape(2, 2, SECOND, split, rows_here)
    twist_real = lax.dynamic_slice_in_dim(tables[2], block_start, blocks, 0)[..., None]
    twist_imag = lax.dynamic_slice_in_dim(tables[3], block_start, blocks, 0)[..., None]
    section_one = complex_times(
        contract("khzrx,wzbhr->wkbx", stacked, inner_split), twist_real, -twist_imag
    )
    section_one = section_one.astype(jnp.bfloat16)
    outer_count = patch_len // SECOND
    outer_ids = (offset_rows // SECOND + jnp.arange(outer_count, dtype=jnp.int32)) % FIRST
    patch_outer = jnp.take(tables[0][0], outer_ids, axis=1)
    gathered = lax.all_gather(section_one, "dir", axis=1, tiled=True)
    depth = gathered.shape[0] * gathered.shape[1]
    patch_matrix = jnp.transpose(patch_outer, (1, 0, 2)).reshape(outer_count, depth)
    phase_patch = jnp.dot(
        patch_matrix, gathered.reshape(depth, -1), preferred_element_type=jnp.float32
    )
    phase_patch = phase_patch.reshape(patch_len, columns) * (1.0 / N)
    screen_field = propagate_columns(phase_patch, tables_y, slant_factor, fresnel_y)
    stacked_field = screen_field.reshape(2, row_count, ROWS_DEV, columns)
    portion = lax.all_to_all(stacked_field, "row", split_axis=1, concat_axis=3, tiled=True)
    item_count = portion.shape[2]
    stacked = portion.reshape(2, item_count, FIRST, SECOND)
    spectral = forward_axis(stacked, tables, fresnel_x, row_patterns, False)
    wave_field = inverse_axis(spectral, tables, row_patterns, False)
    intensity = wave_field[0] * wave_field[0] + wave_field[1] * wave_field[1]
    intensity = intensity.reshape(item_count, XTILES, TILE_X)
    tile_one = jnp.sum(intensity, axis=2)
    tile_two = jnp.sum(intensity * intensity, axis=2)
    tile_rows = ROWS_DEV // YTILES
    first_moment = jnp.sum(tile_one.reshape(YTILES, tile_rows, XTILES), axis=1)
    second_moment = jnp.sum(tile_two.reshape(YTILES, tile_rows, XTILES), axis=1)
    fluctuation, faded_power = tile_statistics(first_moment, second_moment, window[0], tile_rows)
    tile_total = faded_power.shape[0] * faded_power.shape[1]
    local_tile = tile_map[0] - lax.axis_index("row") * tile_total
    inside = (local_tile >= 0) & (local_tile < tile_total)
    tile_row = local_tile // XTILES
    tile_column = local_tile % XTILES
    pick_row = (tile_row[:, None] == jnp.arange(YTILES, dtype=jnp.int32)[None, :]).astype(jnp.float32)
    row_values = jnp.dot(pick_row, faded_power, precision=lax.Precision.HIGHEST)
    pick_column = tile_column[:, None] == jnp.arange(XTILES, dtype=jnp.int32)[None, :]
    looked = jnp.sum(jnp.where(pick_column, row_values, 0.0), axis=1)
    looked = jnp.where(inside, looked, 0.0)
    received = link_gain[0] * looked
    direction = lax.axis_index("dir")
    serves_here = serving == direction
    signal_part = jnp.where(serves_here, received, 0.0)
    interference_part = jnp.where(serves_here, 0.0, received)
    dir_count = lax.axis_size("dir")
    share_size = serving.shape[0] // (dir_count * row_count)
    parts = jnp.stack([signal_part, interference_part]).reshape(2, dir_count, row_count, share_size)
    parts = lax.all_to_all(parts, "row", split_axis=2, concat_axis=2, tiled=True)
    parts = jnp.sum(parts, axis=2, keepdims=True)
    parts = lax.all_to_all(parts, "dir", split_axis=1, concat_axis=1, tiled=True)
    parts = jnp.sum(parts, axis=(1, 2))
    signal, interference = parts[0], parts[1]
    signal_ratio = jnp.log10(signal / (interference + noise_floor))
    return (fluctuation[None], signal_ratio)


def solution(mesh):
    return jax.shard_map(
        body,
        mesh=mesh,
        in_specs=(
            P(None, ("dir", "row"), None),
            P("dir", None),
            P("dir"),
            P("dir", None),
            P("dir", None),
            P(),
        ),
        out_specs=(P("dir", "row", None), P(("dir", "row"))),
        check_vma=False,
    )
```

```python
import math

import jax
import jax.numpy as jnp
from jax import lax
from jax.sharding import PartitionSpec as P

N = 8192
FIRST = 64
SECOND = 128
ROWS_DEV = 32
XTILES = 128
YTILES = 8
TILE_X = 64


full_turn = 2.0 * math.pi
noise_floor = 0.05
tiny_value = 1e-06
strength = 1.6
row_patterns = (
    "zrab,zwak->wrkb",
    "zrkb,zwbc->wrkc",
    "zrkc,wzbc->wrkb",
    "zrkb,wzak->wrab",
    "zrkb,zak->rab",
)
column_patterns = (
    "zaby,zwak->wkby",
    "zkby,zwbc->wkcy",
    "zkcy,wzbc->wkby",
    "zkby,wzak->waby",
    "zkby,zak->aby",
)


def complex_block(real_part, imag_part):
    return jnp.stack(
        [jnp.stack([real_part, imag_part]), jnp.stack([-imag_part, real_part])]
    ).astype(jnp.bfloat16)


def transform_tables(first, second):
    total = first * second
    outer_ids = jnp.arange(first, dtype=jnp.int32)
    inner_ids = jnp.arange(second, dtype=jnp.int32)
    outer_angle = (outer_ids[:, None] * outer_ids[None, :] % first).astype(jnp.float32) * (
        full_turn / first
    )
    inner_angle = (inner_ids[:, None] * inner_ids[None, :] % second).astype(jnp.float32) * (
        full_turn / second
    )
    twist_angle = (outer_ids[:, None] * inner_ids[None, :] % total).astype(jnp.float32) * (
        full_turn / total
    )
    return (
        complex_block(jnp.cos(outer_angle), -jnp.sin(outer_angle)),
        complex_block(jnp.cos(inner_angle), -jnp.sin(inner_angle)),
        jnp.cos(twist_angle),
        -jnp.sin(twist_angle),
    )


def signed_wave(positions, first, second):
    total = first * second
    wave_number = positions // second + first * (positions % second)
    return jnp.where(wave_number >= total // 2, wave_number - total, wave_number).astype(
        jnp.float32
    )


def spectral_filter(row_ids, column_ids):
    wave_rows = signed_wave(row_ids, FIRST, SECOND)
    wave_columns = signed_wave(column_ids, FIRST, SECOND)
    squared_radius = 16.0 + wave_rows[:, None] ** 2 + wave_columns[None, :] ** 2
    return strength * float(N) * float(N) * squared_radius ** (-0.75)


def fresnel_factor(geometry_row, first, second):
    total = first * second
    fresnel_area = 144.0 * jnp.exp2(geometry_row[0].astype(jnp.float32))
    positions = jnp.arange(total, dtype=jnp.int32).reshape(first, second)
    scaled = signed_wave(positions, first, second) * (full_turn / total)
    turning = 0.5 * scaled * scaled * fresnel_area
    return (jnp.cos(turning), -jnp.sin(turning))


def complex_times(values, real_part, imag_part):
    return jnp.stack(
        [
            values[0] * real_part - values[1] * imag_part,
            values[0] * imag_part + values[1] * real_part,
        ]
    )


def contract(pattern, operand, matrix):
    return jnp.einsum(pattern, operand, matrix, preferred_element_type=jnp.float32)


def table_length(tables):
    return tables[0].shape[2] * tables[1].shape[2]


def forward_axis(values, tables, factor, patterns, trailing):
    outer_table, inner_table, twist_real, twist_imag = tables
    factor_real, factor_imag = factor
    if trailing:
        twist_real, twist_imag = (twist_real[..., None], twist_imag[..., None])
        factor_real, factor_imag = (factor_real[..., None], factor_imag[..., None])
    section_one = complex_times(
        contract(patterns[0], values, outer_table), twist_real, twist_imag
    ).astype(jnp.bfloat16)
    section_two = contract(patterns[1], section_one, inner_table)
    return complex_times(section_two, factor_real, factor_imag).astype(jnp.bfloat16)


def inverse_first(values, tables, patterns, trailing):
    outer_table, inner_table, twist_real, twist_imag = tables
    if trailing:
        twist_real, twist_imag = (twist_real[..., None], twist_imag[..., None])
    return complex_times(
        contract(patterns[2], values, inner_table), twist_real, -twist_imag
    ).astype(jnp.bfloat16)


def inverse_axis(values, tables, patterns, trailing):
    section_one = inverse_first(values, tables, patterns, trailing)
    return contract(patterns[3], section_one, tables[0]) * (1.0 / table_length(tables))


def window_matrix(half_width):
    positions = jnp.arange(XTILES, dtype=jnp.int32)
    difference = (positions[:, None] - positions[None, :]) % XTILES
    distance = jnp.minimum(difference, XTILES - difference)
    return (distance <= half_width).astype(jnp.float32)


def tile_statistics(first_moment, second_moment, half_width, tile_rows):
    window_mask = window_matrix(half_width)
    cells = ((2 * half_width + 1) * (TILE_X * tile_rows)).astype(jnp.float32)
    mean_one = jnp.dot(first_moment, window_mask, precision=lax.Precision.HIGHEST) / cells
    mean_two = jnp.dot(second_moment, window_mask, precision=lax.Precision.HIGHEST) / cells
    fluctuation = mean_two / (mean_one * mean_one + tiny_value) - 1.0
    return (fluctuation, mean_one * jnp.exp(-fluctuation))


def turn_pair(angle):
    quarter = jnp.round(angle * (2.0 / 3.141592653589793))
    rest = angle - quarter * 1.5703125
    rest = rest - quarter * 4.837512969970703125e-4
    rest = rest - quarter * 7.54978995489188216e-8
    square = rest * rest
    sine = rest + rest * square * (
        -1.6666654611e-1 + square * (8.3321608736e-3 + square * -1.9515295891e-4)
    )
    cosine = 1.0 - 0.5 * square + square * square * (
        4.166664568298827e-2 + square * (-1.388731625493765e-3 + square * 2.443315711809948e-5)
    )
    turn = quarter.astype(jnp.int32) & 3
    swap = (turn & 1) == 1
    sin_value = jnp.where(swap, cosine, sine)
    cos_value = jnp.where(swap, sine, cosine)
    sin_value = jnp.where(turn >= 2, -sin_value, sin_value)
    cos_value = jnp.where((turn == 1) | (turn == 2), -cos_value, cos_value)
    return cos_value, sin_value


def propagate_columns(phase_patch, tables_y, slant_factor, fresnel_y):
    patch_rows = phase_patch.shape[0]
    width_here = phase_patch.shape[1]
    outer_len = tables_y[0].shape[2]
    inner_len = tables_y[1].shape[2]
    turned_phase = slant_factor * phase_patch
    screen_field = jnp.stack(turn_pair(turned_phase)).astype(jnp.bfloat16)
    stacked = screen_field.reshape(2, outer_len, inner_len, width_here)
    spectral = forward_axis(stacked, tables_y, fresnel_y, column_patterns, True)
    result = inverse_axis(spectral, tables_y, column_patterns, True)
    return result.astype(jnp.bfloat16).reshape(2, patch_rows, width_here)


def body(white_noise, geometry, window, tile_map, link_gain, serving):
    row_count = lax.axis_size("row")
    tables = transform_tables(FIRST, SECOND)
    tables_y = transform_tables(row_count, ROWS_DEV)
    patch_len = row_count * ROWS_DEV
    rows_here = white_noise.shape[1]
    row_start = lax.axis_index(("dir", "row")) * rows_here
    row_ids = row_start + jnp.arange(rows_here, dtype=jnp.int32)
    column_ids = jnp.arange(N, dtype=jnp.int32)
    spectral_gain = spectral_filter(row_ids, column_ids)
    spectrum = (white_noise.astype(jnp.float32) * spectral_gain).astype(jnp.bfloat16)
    section_first = inverse_first(
        spectrum.reshape(2, rows_here, FIRST, SECOND), tables, row_patterns, False
    )
    half_screen = contract("zrkb,wzak->awrb", section_first, tables[0]) * (1.0 / N)
    half_screen = half_screen.astype(jnp.bfloat16)
    turned = lax.all_to_all(half_screen, "row", split_axis=0, concat_axis=0, tiled=True)
    slant_factor = 1.0 + 0.25 * geometry[0, 1].astype(jnp.float32)
    fresnel_x = fresnel_factor(geometry[0], FIRST, SECOND)
    fresnel_y = fresnel_factor(geometry[0], row_count, ROWS_DEV)
    offset_rows = N // 4 * geometry[0, 1]
    columns = SECOND
    blocks = row_count * rows_here // SECOND
    split = SECOND // rows_here
    block_start = lax.axis_index("dir") * blocks
    stacked = turned.reshape(blocks, split, 2, rows_here, columns)
    inner_split = tables[1].reshape(2, 2, SECOND, split, rows_here)
    twist_real = lax.dynamic_slice_in_dim(tables[2], block_start, blocks, 0)[..., None]
    twist_imag = lax.dynamic_slice_in_dim(tables[3], block_start, blocks, 0)[..., None]
    section_one = complex_times(
        contract("khzrx,wzbhr->wkbx", stacked, inner_split), twist_real, -twist_imag
    )
    section_one = section_one.astype(jnp.bfloat16)
    outer_count = patch_len // SECOND
    outer_ids = (offset_rows // SECOND + jnp.arange(outer_count, dtype=jnp.int32)) % FIRST
    patch_outer = jnp.take(tables[0][0], outer_ids, axis=1)
    gathered = lax.all_gather(section_one, "dir", axis=1, tiled=True)
    depth = gathered.shape[0] * gathered.shape[1]
    patch_matrix = jnp.transpose(patch_outer, (1, 0, 2)).reshape(outer_count, depth)
    phase_patch = jnp.dot(
        patch_matrix, gathered.reshape(depth, -1), preferred_element_type=jnp.float32
    )
    phase_patch = phase_patch.reshape(patch_len, columns) * (1.0 / N)
    screen_field = propagate_columns(phase_patch, tables_y, slant_factor, fresnel_y)
    stacked_field = screen_field.reshape(2, row_count, ROWS_DEV, columns)
    portion = lax.all_to_all(stacked_field, "row", split_axis=1, concat_axis=3, tiled=True)
    item_count = portion.shape[2]
    stacked = portion.reshape(2, item_count, FIRST, SECOND)
    spectral = forward_axis(stacked, tables, fresnel_x, row_patterns, False)
    wave_field = inverse_axis(spectral, tables, row_patterns, False)
    intensity = wave_field[0] * wave_field[0] + wave_field[1] * wave_field[1]
    intensity = intensity.reshape(item_count, XTILES, TILE_X)
    tile_one = jnp.sum(intensity, axis=2)
    tile_two = jnp.sum(intensity * intensity, axis=2)
    tile_rows = ROWS_DEV // YTILES
    first_moment = jnp.sum(tile_one.reshape(YTILES, tile_rows, XTILES), axis=1)
    second_moment = jnp.sum(tile_two.reshape(YTILES, tile_rows, XTILES), axis=1)
    fluctuation, faded_power = tile_statistics(first_moment, second_moment, window[0], tile_rows)
    tile_total = faded_power.shape[0] * faded_power.shape[1]
    local_tile = tile_map[0] - lax.axis_index("row") * tile_total
    inside = (local_tile >= 0) & (local_tile < tile_total)
    tile_row = local_tile // XTILES
    tile_column = local_tile % XTILES
    pick_row = (tile_row[:, None] == jnp.arange(YTILES, dtype=jnp.int32)[None, :]).astype(jnp.float32)
    row_values = jnp.dot(pick_row, faded_power, precision=lax.Precision.HIGHEST)
    pick_column = tile_column[:, None] == jnp.arange(XTILES, dtype=jnp.int32)[None, :]
    looked = jnp.sum(jnp.where(pick_column, row_values, 0.0), axis=1)
    looked = jnp.where(inside, looked, 0.0)
    received = link_gain[0] * looked
    direction = lax.axis_index("dir")
    serves_here = serving == direction
    signal_part = jnp.where(serves_here, received, 0.0)
    interference_part = jnp.where(serves_here, 0.0, received)
    dir_count = lax.axis_size("dir")
    share_size = serving.shape[0] // (dir_count * row_count)
    parts = jnp.stack([signal_part, interference_part]).reshape(2, dir_count, row_count, share_size)
    parts = lax.all_to_all(parts, "row", split_axis=2, concat_axis=2, tiled=True)
    parts = jnp.sum(parts, axis=2, keepdims=True)
    parts = lax.all_to_all(parts, "dir", split_axis=1, concat_axis=1, tiled=True)
    parts = jnp.sum(parts, axis=(1, 2))
    signal, interference = parts[0], parts[1]
    signal_ratio = jnp.log10(signal / (interference + noise_floor))
    return (fluctuation[None], signal_ratio)


def solution(mesh):
    return jax.shard_map(
        body,
        mesh=mesh,
        in_specs=(
            P(None, ("dir", "row"), None),
            P("dir", None),
            P("dir"),
            P("dir", None),
            P("dir", None),
            P(),
        ),
        out_specs=(P("dir", "row", None), P(("dir", "row"))),
        check_vma=False,
    )
```

```python
import math

import jax
import jax.numpy as jnp
from jax import lax
from jax.sharding import PartitionSpec as P

N = 8192
FIRST = 64
SECOND = 128
ROWS_DEV = 32
XTILES = 128
YTILES = 8
TILE_X = 64


full_turn = 2.0 * math.pi
noise_floor = 0.05
tiny_value = 1e-06
strength = 1.6
row_patterns = (
    "zrab,zwak->wrkb",
    "zrkb,zwbc->wrkc",
    "zrkc,wzbc->wrkb",
    "zrkb,wzak->wrab",
    "zrkb,zak->rab",
)
column_patterns = (
    "zaby,zwak->wkby",
    "zkby,zwbc->wkcy",
    "zkcy,wzbc->wkby",
    "zkby,wzak->waby",
    "zkby,zak->aby",
)


def complex_block(real_part, imag_part):
    return jnp.stack(
        [jnp.stack([real_part, imag_part]), jnp.stack([-imag_part, real_part])]
    ).astype(jnp.bfloat16)


def transform_tables(first, second):
    total = first * second
    outer_ids = jnp.arange(first, dtype=jnp.int32)
    inner_ids = jnp.arange(second, dtype=jnp.int32)
    outer_angle = (outer_ids[:, None] * outer_ids[None, :] % first).astype(jnp.float32) * (
        full_turn / first
    )
    inner_angle = (inner_ids[:, None] * inner_ids[None, :] % second).astype(jnp.float32) * (
        full_turn / second
    )
    twist_angle = (outer_ids[:, None] * inner_ids[None, :] % total).astype(jnp.float32) * (
        full_turn / total
    )
    return (
        complex_block(jnp.cos(outer_angle), -jnp.sin(outer_angle)),
        complex_block(jnp.cos(inner_angle), -jnp.sin(inner_angle)),
        jnp.cos(twist_angle),
        -jnp.sin(twist_angle),
    )


def signed_wave(positions, first, second):
    total = first * second
    wave_number = positions // second + first * (positions % second)
    return jnp.where(wave_number >= total // 2, wave_number - total, wave_number).astype(
        jnp.float32
    )


def spectral_filter(row_ids, column_ids):
    wave_rows = signed_wave(row_ids, FIRST, SECOND)
    wave_columns = signed_wave(column_ids, FIRST, SECOND)
    squared_radius = 16.0 + wave_rows[:, None] ** 2 + wave_columns[None, :] ** 2
    return strength * float(N) * float(N) * squared_radius ** (-0.75)


def fresnel_factor(geometry_row, first, second):
    total = first * second
    fresnel_area = 144.0 * jnp.exp2(geometry_row[0].astype(jnp.float32))
    positions = jnp.arange(total, dtype=jnp.int32).reshape(first, second)
    scaled = signed_wave(positions, first, second) * (full_turn / total)
    turning = 0.5 * scaled * scaled * fresnel_area
    return (jnp.cos(turning), -jnp.sin(turning))


def complex_times(values, real_part, imag_part):
    return jnp.stack(
        [
            values[0] * real_part - values[1] * imag_part,
            values[0] * imag_part + values[1] * real_part,
        ]
    )


def contract(pattern, operand, matrix):
    return jnp.einsum(pattern, operand, matrix, preferred_element_type=jnp.float32)


def table_length(tables):
    return tables[0].shape[2] * tables[1].shape[2]


def forward_axis(values, tables, factor, patterns, trailing):
    outer_table, inner_table, twist_real, twist_imag = tables
    factor_real, factor_imag = factor
    if trailing:
        twist_real, twist_imag = (twist_real[..., None], twist_imag[..., None])
        factor_real, factor_imag = (factor_real[..., None], factor_imag[..., None])
    section_one = complex_times(
        contract(patterns[0], values, outer_table), twist_real, twist_imag
    ).astype(jnp.bfloat16)
    section_two = contract(patterns[1], section_one, inner_table)
    return complex_times(section_two, factor_real, factor_imag).astype(jnp.bfloat16)


def inverse_first(values, tables, patterns, trailing):
    outer_table, inner_table, twist_real, twist_imag = tables
    if trailing:
        twist_real, twist_imag = (twist_real[..., None], twist_imag[..., None])
    return complex_times(
        contract(patterns[2], values, inner_table), twist_real, -twist_imag
    ).astype(jnp.bfloat16)


def inverse_axis(values, tables, patterns, trailing):
    section_one = inverse_first(values, tables, patterns, trailing)
    return contract(patterns[3], section_one, tables[0]) * (1.0 / table_length(tables))


def window_matrix(half_width):
    positions = jnp.arange(XTILES, dtype=jnp.int32)
    difference = (positions[:, None] - positions[None, :]) % XTILES
    distance = jnp.minimum(difference, XTILES - difference)
    return (distance <= half_width).astype(jnp.float32)


def tile_statistics(first_moment, second_moment, half_width, tile_rows):
    window_mask = window_matrix(half_width)
    cells = ((2 * half_width + 1) * (TILE_X * tile_rows)).astype(jnp.float32)
    mean_one = jnp.dot(first_moment, window_mask, precision=lax.Precision.HIGHEST) / cells
    mean_two = jnp.dot(second_moment, window_mask, precision=lax.Precision.HIGHEST) / cells
    fluctuation = mean_two / (mean_one * mean_one + tiny_value) - 1.0
    return (fluctuation, mean_one * jnp.exp(-fluctuation))


def turn_pair(angle):
    quarter = jnp.round(angle * (2.0 / 3.141592653589793))
    rest = angle - quarter * 1.5703125
    rest = rest - quarter * 4.837512969970703125e-4
    rest = rest - quarter * 7.54978995489188216e-8
    square = rest * rest
    sine = rest + rest * square * (
        -1.6666654611e-1 + square * (8.3321608736e-3 + square * -1.9515295891e-4)
    )
    cosine = 1.0 - 0.5 * square + square * square * (
        4.166664568298827e-2 + square * (-1.388731625493765e-3 + square * 2.443315711809948e-5)
    )
    turn = quarter.astype(jnp.int32) & 3
    swap = (turn & 1) == 1
    sin_value = jnp.where(swap, cosine, sine)
    cos_value = jnp.where(swap, sine, cosine)
    sin_value = jnp.where(turn >= 2, -sin_value, sin_value)
    cos_value = jnp.where((turn == 1) | (turn == 2), -cos_value, cos_value)
    return cos_value, sin_value


def propagate_columns(phase_patch, tables_y, slant_factor, fresnel_y):
    patch_rows = phase_patch.shape[0]
    width_here = phase_patch.shape[1]
    outer_len = tables_y[0].shape[2]
    inner_len = tables_y[1].shape[2]
    turned_phase = slant_factor * phase_patch
    screen_field = jnp.stack(turn_pair(turned_phase)).astype(jnp.bfloat16)
    stacked = screen_field.reshape(2, outer_len, inner_len, width_here)
    spectral = forward_axis(stacked, tables_y, fresnel_y, column_patterns, True)
    result = inverse_axis(spectral, tables_y, column_patterns, True)
    return result.astype(jnp.bfloat16).reshape(2, patch_rows, width_here)


def body(white_noise, geometry, window, tile_map, link_gain, serving):
    row_count = lax.axis_size("row")
    tables = transform_tables(FIRST, SECOND)
    tables_y = transform_tables(row_count, ROWS_DEV)
    patch_len = row_count * ROWS_DEV
    rows_here = white_noise.shape[1]
    row_start = lax.axis_index(("dir", "row")) * rows_here
    row_ids = row_start + jnp.arange(rows_here, dtype=jnp.int32)
    column_ids = jnp.arange(N, dtype=jnp.int32)
    spectral_gain = spectral_filter(row_ids, column_ids)
    spectrum = (white_noise.astype(jnp.float32) * spectral_gain).astype(jnp.bfloat16)
    section_first = inverse_first(
        spectrum.reshape(2, rows_here, FIRST, SECOND), tables, row_patterns, False
    )
    half_screen = contract("zrkb,wzak->awrb", section_first, tables[0]) * (1.0 / N)
    half_screen = half_screen.astype(jnp.bfloat16)
    turned = lax.all_to_all(half_screen, "row", split_axis=0, concat_axis=0, tiled=True)
    slant_factor = 1.0 + 0.25 * geometry[0, 1].astype(jnp.float32)
    fresnel_x = fresnel_factor(geometry[0], FIRST, SECOND)
    fresnel_y = fresnel_factor(geometry[0], row_count, ROWS_DEV)
    offset_rows = N // 4 * geometry[0, 1]
    columns = SECOND
    blocks = row_count * rows_here // SECOND
    split = SECOND // rows_here
    block_start = lax.axis_index("dir") * blocks
    stacked = turned.reshape(blocks, split, 2, rows_here, columns)
    inner_split = tables[1].reshape(2, 2, SECOND, split, rows_here)
    twist_real = lax.dynamic_slice_in_dim(tables[2], block_start, blocks, 0)[..., None]
    twist_imag = lax.dynamic_slice_in_dim(tables[3], block_start, blocks, 0)[..., None]
    section_one = complex_times(
        contract("khzrx,wzbhr->wkbx", stacked, inner_split), twist_real, -twist_imag
    )
    section_one = section_one.astype(jnp.bfloat16)
    outer_count = patch_len // SECOND
    outer_ids = (offset_rows // SECOND + jnp.arange(outer_count, dtype=jnp.int32)) % FIRST
    patch_outer = jnp.take(tables[0][0], outer_ids, axis=1)
    gathered = lax.all_gather(section_one, "dir", axis=1, tiled=True)
    depth = gathered.shape[0] * gathered.shape[1]
    patch_matrix = jnp.transpose(patch_outer, (1, 0, 2)).reshape(outer_count, depth)
    phase_patch = jnp.dot(
        patch_matrix, gathered.reshape(depth, -1), preferred_element_type=jnp.float32
    )
    phase_patch = phase_patch.reshape(patch_len, columns) * (1.0 / N)
    screen_field = propagate_columns(phase_patch, tables_y, slant_factor, fresnel_y)
    stacked_field = screen_field.reshape(2, row_count, ROWS_DEV, columns)
    portion = lax.all_to_all(stacked_field, "row", split_axis=1, concat_axis=3, tiled=True)
    item_count = portion.shape[2]
    stacked = portion.reshape(2, item_count, FIRST, SECOND)
    spectral = forward_axis(stacked, tables, fresnel_x, row_patterns, False)
    wave_field = inverse_axis(spectral, tables, row_patterns, False)
    intensity = wave_field[0] * wave_field[0] + wave_field[1] * wave_field[1]
    intensity = intensity.reshape(item_count, XTILES, TILE_X)
    tile_one = jnp.sum(intensity, axis=2)
    tile_two = jnp.sum(intensity * intensity, axis=2)
    tile_rows = ROWS_DEV // YTILES
    first_moment = jnp.sum(tile_one.reshape(YTILES, tile_rows, XTILES), axis=1)
    second_moment = jnp.sum(tile_two.reshape(YTILES, tile_rows, XTILES), axis=1)
    fluctuation, faded_power = tile_statistics(first_moment, second_moment, window[0], tile_rows)
    tile_total = faded_power.shape[0] * faded_power.shape[1]
    local_tile = tile_map[0] - lax.axis_index("row") * tile_total
    inside = (local_tile >= 0) & (local_tile < tile_total)
    tile_row = local_tile // XTILES
    tile_column = local_tile % XTILES
    pick_row = (tile_row[:, None] == jnp.arange(YTILES, dtype=jnp.int32)[None, :]).astype(jnp.bfloat16)
    high_part = faded_power.astype(jnp.bfloat16)
    middle_rest = faded_power - high_part.astype(jnp.float32)
    middle_part = middle_rest.astype(jnp.bfloat16)
    low_part = (middle_rest - middle_part.astype(jnp.float32)).astype(jnp.bfloat16)
    split_parts = jnp.concatenate([high_part, middle_part, low_part], axis=1)
    row_parts = jnp.dot(pick_row, split_parts, preferred_element_type=jnp.float32)
    row_parts = row_parts.reshape(-1, 3, XTILES)
    row_values = (row_parts[:, 0] + row_parts[:, 1]) + row_parts[:, 2]
    pick_column = tile_column[:, None] == jnp.arange(XTILES, dtype=jnp.int32)[None, :]
    looked = jnp.sum(jnp.where(pick_column, row_values, 0.0), axis=1)
    looked = jnp.where(inside, looked, 0.0)
    received = link_gain[0] * looked
    direction = lax.axis_index("dir")
    serves_here = serving == direction
    signal_part = jnp.where(serves_here, received, 0.0)
    interference_part = jnp.where(serves_here, 0.0, received)
    dir_count = lax.axis_size("dir")
    share_size = serving.shape[0] // (dir_count * row_count)
    parts = jnp.stack([signal_part, interference_part]).reshape(2, dir_count, row_count, share_size)
    parts = lax.all_to_all(parts, "row", split_axis=2, concat_axis=2, tiled=True)
    parts = jnp.sum(parts, axis=2, keepdims=True)
    parts = lax.all_to_all(parts, "dir", split_axis=1, concat_axis=1, tiled=True)
    parts = jnp.sum(parts, axis=(1, 2))
    signal, interference = parts[0], parts[1]
    signal_ratio = jnp.log10(signal / (interference + noise_floor))
    return (fluctuation[None], signal_ratio)


def solution(mesh):
    return jax.shard_map(
        body,
        mesh=mesh,
        in_specs=(
            P(None, ("dir", "row"), None),
            P("dir", None),
            P("dir"),
            P("dir", None),
            P("dir", None),
            P(),
        ),
        out_specs=(P("dir", "row", None), P(("dir", "row"))),
        check_vma=False,
    )
```
